128 devices in a mesh: ctx: 16 (over y, x), exp: 8 (over z, core).
Axes of the slice: x: 4, y: 4, z: 4, core: 2. Of those that a mesh axis runs over, the one named last changes fastest.
Arguments:
- queries: bfloat16 [8192, 8192], P('ctx', 'exp'), may hold values from -6 to 6
- keys: bfloat16 [8192, 8192], P('ctx', 'exp'), may hold values from -6 to 6
- values: bfloat16 [8192, 8192], P('ctx', 'exp'), may hold values from -6 to 6
- log_decay: float32 [8192, 64], P('ctx', 'exp'), may hold values from -2 to 0, as said below
- residual: bfloat16 [8192, 3072], P(('ctx', 'exp')), may hold values from -6 to 6
- out_proj: bfloat16 [8192, 3072], P('exp'), may hold values from -0.0625 to 0.0625
- expert_ids: int32 [8192, 2], P(('ctx', 'exp')), may hold values from 0 to 15, all different within a row; in each aligned block of 64 rows (0 to 63, 64 to 127, ...) at most 10 rows name the same one
- route_weights: float32 [8192, 2], P(('ctx', 'exp')), may hold values from 0.1 to 0.9
- w_gate: bfloat16 [16, 3072, 6144], P('exp', None, 'ctx'), may hold values from -0.109375 to 0.109375
- w_up: bfloat16 [16, 3072, 6144], P('exp', None, 'ctx'), may hold values from -0.109375 to 0.109375
- w_down: bfloat16 [16, 6144, 3072], P('exp', 'ctx'), may hold values from -0.078125 to 0.078125
Outputs:
- mixed: bfloat16 [8192, 3072], P(('ctx', 'exp'))
The draws below stay inside these ranges and needn't reach their ends.
Inputs may be any that keep to these rules, and one draw needn't show every extreme that they name: `expert_ids`: each token names two different experts. In each aligned block of 64 tokens no expert is named more than 10 times, and in some blocks one expert is named exactly 10 times. `log_decay`: every entry is negative.
All inputs are finite; a program needn't handle non-finite values.
Results may differ from the reference program's by a relative error of at most 0.019.
Values may be sent and summed in bfloat16 or wider, within the bound.
No kernel may reach another device: no remote copies, remote signals or barrier semaphores. Data moves between devices by JAX's collectives and lax.ppermute only.
A program may use at most 128 MiB of HBM per device.

```python
import math
import jax
import jax.numpy as jnp
import numpy as np
from jax import lax

D = 3072
HEADS = 64
HD = 128
EXPERTS = 16
FF = 6144
TOK_DEV = 512
TOKENS = 8192
MTOK = 64
CAP = 10
N_CTX = 16
N_EXP = 8


def draw_log_decay(key, part):
    keys_all = jax.random.split(jax.random.fold_in(key, 7717), 7)
    picks = jax.random.randint(keys_all[0], (HEADS,), 0, 16)
    fast = picks < 8
    fast_rate = jnp.exp(jax.random.uniform(keys_all[1], (HEADS,), jnp.float32, math.log(1.0 / 50.0), math.log(1.0 / 30.0)))
    slow_rate = jnp.exp(jax.random.uniform(keys_all[2], (HEADS,), jnp.float32, math.log(0.05), math.log(0.3))) / TOKENS
    base = jnp.where(fast, fast_rate, slow_rate)
    block_count = TOKENS // TOK_DEV
    block_factor = jnp.exp(jax.random.uniform(keys_all[3], (block_count, HEADS), jnp.float32, math.log(0.6), math.log(1.5)))
    token_factor = jnp.exp(jax.random.uniform(keys_all[4], (TOKENS, HEADS), jnp.float32, math.log(0.5), math.log(1.5)))
    forgetting_factor = base[None, :] * jnp.repeat(block_factor, TOK_DEV, axis=0) * token_factor
    spots = jax.random.randint(keys_all[5], (2, HEADS), 0, TOKENS)
    layer_number = jax.random.uniform(keys_all[6], (2, HEADS), jnp.float32, 0.2, 0.5)
    place = jnp.arange(TOKENS, dtype=jnp.int32)
    assignment_tally = place[:, None, None] == spots[None, :, :]
    sequence_pieces = jnp.sum(jnp.where(assignment_tally, jnp.log(1.0 - layer_number)[None, :, :], 0.0), axis=1)
    return (sequence_pieces - forgetting_factor).astype(jnp.float32)


def steps_of(rng, dims, pieces, low, high):
    level, own = 1.0, jax.random.fold_in(rng, 6)
    for position, shards_of in pieces:
        draws = jnp.exp(jax.random.uniform(jax.random.fold_in(own, position), (shards_of,), jnp.float32, low / len(pieces), high / len(pieces)))
        level = level * jnp.repeat(draws, dims[position] // shards_of).reshape([-1 if axis == position else 1 for axis in range(len(dims))])
    return level


def assign_block(own_key, own, number, rows, amount, top, bound, slope):
    order = jax.random.permutation(own_key, amount)
    crowded, ordinary = portions_of(amount, rows * top, bound, slope, True), portions_of(amount, rows * top, bound, slope, False)
    places = jnp.arange(amount)

    def named(lengths, turn):
        used = int((lengths > 0).sum())
        fixed = max(1, used // 4)
        shifted = fixed + (places - fixed + turn * (used - fixed)) % max(1, amount - fixed)
        return jnp.zeros((amount,), jnp.int32).at[order[jnp.where(places < fixed, places, shifted)]].set(jnp.asarray(lengths, jnp.int32))

    lengths = jnp.where(number % 4 == 0, named(crowded, number // 4), named(ordinary, number - number // 4 - 1))
    mixed = jax.random.permutation(jax.random.fold_in(own, 3), amount)
    donor, sink = mixed[0:amount // 2 * 2:2], mixed[1:amount // 2 * 2:2]
    room = jnp.minimum(lengths[donor] - 1, bound - lengths[sink]) // 2
    room = jnp.where((donor == order[0]) | (sink == order[0]) | (lengths[sink] == 0), 0, jnp.maximum(room, 0))
    shifted = jax.random.randint(jax.random.fold_in(own, 4), (amount // 2,), 0, 1 << 20) % (room + 1)
    lengths = lengths.at[donor].add(-shifted).at[sink].add(shifted)
    members = jnp.searchsorted(jnp.cumsum(lengths), jnp.arange(rows * top), side="right").astype(jnp.int32)
    grid = members.reshape(top, rows).T
    grid = grid[jax.random.permutation(jax.random.fold_in(own, 1), rows)]
    turn = jax.random.randint(jax.random.fold_in(own, 2), (rows, 1), 0, top)
    return jnp.take_along_axis(grid, (jnp.arange(top)[None, :] + turn) % top, axis=1)


def portions_of(amount, total, most, lean, full):
    portions = [(1 << 20) // math.isqrt(rank ** lean) + 1 for rank in range(1, amount + 1)]
    largest = most if full else min(most, max(-(-total // amount), total * portions[0] // sum(portions)))
    least = 1 if total - largest >= amount - 1 else 0
    holding, spare = [largest] + [least] * (amount - 1), total - largest - least * (amount - 1)
    while spare > 0:
        free = [i for i in range(1, amount) if holding[i] < largest] or [i for i in range(1, amount) if holding[i] < most]
        mass, left = sum([portions[i] for i in free]), spare
        for i in free:
            more = min(most - holding[i], max(1, left * portions[i] // mass), spare)
            holding[i] = holding[i] + more
            spare = spare - more
    return np.array(holding)


def gaussian(stream_key, dims, width, most, pieces=(), held_as=jnp.bfloat16):
    drawn = width * jax.random.normal(stream_key, dims, jnp.float32)
    if pieces:
        drawn = drawn * steps_of(stream_key, dims, pieces, -0.22, 0.18)
    return jnp.clip(drawn, -most, most).astype(held_as)


def setup_inputs(seed: int = 0) -> dict:
    streams_of = jax.random.split(jax.random.key(seed), 12)
    queries = gaussian(streams_of[0], (TOKENS, HEADS * HD), 1.0, 6.0, ((0, 16), (1, 8)))
    keys = gaussian(streams_of[1], (TOKENS, HEADS * HD), 1.0, 6.0, ((0, 16), (1, 8)))
    values = gaussian(streams_of[2], (TOKENS, HEADS * HD), 1.0, 6.0, ((0, 16), (1, 8)))
    log_decay = draw_log_decay(jax.random.fold_in(streams_of[11], 71), 0)
    residual = gaussian(streams_of[4], (TOKENS, D), 1.0, 6.0, ((0, 128),))
    out_proj = gaussian(streams_of[5], (HEADS * HD, D), (HEADS * HD) ** -0.5, 0.0625, ((0, 8),))
    expert_ids_keys = jax.random.split(jax.random.fold_in(streams_of[6], 1), TOKENS // MTOK)
    expert_ids_turns = jax.random.permutation(jax.random.fold_in(streams_of[6], 3), TOKENS // MTOK)
    expert_ids = jax.vmap(lambda own, number: assign_block(jax.random.fold_in(streams_of[6], 2), own, number, MTOK, EXPERTS, 2, CAP, 2))(expert_ids_keys, expert_ids_turns).reshape((TOKENS, 2))
    route_weights = jnp.clip(0.1 + 0.79999997 * jax.random.uniform(streams_of[7], (TOKENS, 2), jnp.float32) ** steps_of(streams_of[7], (TOKENS, 2), ((0, 128),), -0.2, 0.2), 0.1, 0.9)
    w_gate = gaussian(streams_of[8], (EXPERTS, D, FF), D ** -0.5, 0.109375, ((0, 8), (2, 16)))
    w_up = gaussian(streams_of[9], (EXPERTS, D, FF), D ** -0.5, 0.109375, ((0, 8), (2, 16)))
    w_down = gaussian(streams_of[10], (EXPERTS, FF, D), FF ** -0.5, 0.078125, ((0, 8), (1, 16)))
    return dict(queries=queries, keys=keys, values=values, log_decay=log_decay, residual=residual, out_proj=out_proj, expert_ids=expert_ids, route_weights=route_weights, w_gate=w_gate, w_up=w_up, w_down=w_down)


EPS = 1e-06

def attend_block(carried, block):
    qb, kb, vb, ab = block
    cum = jnp.cumsum(ab, axis=0)
    qf = qb.astype(jnp.float32)
    kf = kb.astype(jnp.float32)
    vf = vb.astype(jnp.float32)
    scores = jnp.einsum('thd,shd->hts', qf, kf, precision=lax.Precision.HIGHEST)
    place = jnp.arange(qb.shape[0], dtype=jnp.int32)
    causal = (place[:, None] >= place[None, :])[None]
    diff = cum.T[:, :, None] - cum.T[:, None, :]
    weights = jnp.where(causal, scores * jnp.exp(jnp.where(causal, diff, 0.0)), 0.0).astype(jnp.bfloat16)
    intra = jnp.einsum('hts,shd->thd', weights.astype(jnp.float32), vf, precision=lax.Precision.HIGHEST)
    inter = jnp.exp(cum)[:, :, None] * jnp.einsum('thd,hde->the', qf, carried, precision=lax.Precision.HIGHEST)
    attn = intra + inter
    last = cum[-1]
    scaled_keys = (kf * jnp.exp(last[None, :] - cum)[:, :, None]).astype(jnp.bfloat16)
    state = jnp.einsum('thd,the->hde', scaled_keys.astype(jnp.float32), vf, precision=lax.Precision.HIGHEST)
    new_carried = jnp.exp(last)[:, None, None] * carried + state
    normed = (attn * lax.rsqrt(lax.optimization_barrier(jnp.mean(attn * attn, axis=-1, keepdims=True)) + EPS)).astype(jnp.bfloat16)
    return (new_carried, normed)

def reference(queries, keys, values, log_decay, residual, out_proj, expert_ids, route_weights, w_gate, w_up, w_down):
    shaped = (N_CTX, TOK_DEV, HEADS, HD)
    blocks = (queries.reshape(shaped), keys.reshape(shaped), values.reshape(shaped), log_decay.reshape(N_CTX, TOK_DEV, HEADS))
    start_state = jnp.zeros((HEADS, HD, HD), jnp.float32)
    _, normed = lax.scan(attend_block, start_state, blocks)
    normed = normed.reshape(TOKENS, HEADS * HD)
    group = HEADS * HD // N_EXP

    def add_group(total, index):
        begin = (index * group).astype(jnp.int32)
        part = jnp.dot(lax.dynamic_slice_in_dim(normed, begin, group, 1), lax.dynamic_slice_in_dim(out_proj, begin, group, 0), preferred_element_type=jnp.float32).astype(jnp.bfloat16)
        part = lax.optimization_barrier(part)
        return (total + part.astype(jnp.float32), None)
    proj, _ = lax.scan(add_group, jnp.zeros((TOKENS, D), jnp.float32), jnp.arange(N_EXP, dtype=jnp.int32))
    feature_vector = residual.astype(jnp.float32) + proj
    moe_in = (feature_vector * lax.rsqrt(lax.optimization_barrier(jnp.mean(feature_vector * feature_vector, axis=-1, keepdims=True)) + EPS)).astype(jnp.bfloat16)
    flat_ids = expert_ids.reshape(-1)
    most_rows = N_CTX * N_EXP * CAP
    slice_units = FF // N_CTX

    def per_expert(expert):
        order = jnp.argsort(jnp.where(flat_ids == expert, 0, 1).astype(jnp.int32), stable=True)[:most_rows].astype(jnp.int32)
        valid = jnp.take(flat_ids, order) == expert
        rows = jnp.take(moe_in, order // 2, axis=0)
        gate = jnp.dot(rows, w_gate[expert], preferred_element_type=jnp.float32)
        upper = jnp.dot(rows, w_up[expert], preferred_element_type=jnp.float32)
        act = (jax.nn.silu(gate) * upper).astype(jnp.bfloat16)
        parts = jnp.einsum('mcf,cfd->mcd', act.reshape(most_rows, N_CTX, slice_units).astype(jnp.float32), w_down[expert].reshape(N_CTX, slice_units, D).astype(jnp.float32), precision=lax.Precision.HIGHEST)
        parts = lax.optimization_barrier(parts.astype(jnp.bfloat16))
        out = lax.optimization_barrier(jnp.sum(parts.astype(jnp.float32), axis=1)).astype(jnp.bfloat16)
        target = jnp.where(valid, order, 2 * TOKENS).astype(jnp.int32)
        return (target, out)
    target_experts, outs = lax.map(per_expert, jnp.arange(EXPERTS, dtype=jnp.int32))
    expert_out = jnp.zeros((2 * TOKENS, D), jnp.bfloat16).at[target_experts.reshape(-1)].set(outs.reshape(-1, D), mode='drop')
    expert_out = expert_out.astype(jnp.float32).reshape(TOKENS, 2, D)
    moe = route_weights[:, 0:1] * expert_out[:, 0] + route_weights[:, 1:2] * expert_out[:, 1]
    return (feature_vector + moe).astype(jnp.bfloat16)
```

```python
import jax
import jax.numpy as jnp
from jax import lax
from jax.sharding import PartitionSpec as P

EPS = 1e-06


def exclusive_scan(rate, state, axis):
    length = lax.axis_size(axis)
    first = [(i, i + 1) for i in range(length - 1)]
    r = lax.ppermute(rate, axis, first)
    s = lax.ppermute(state.astype(jnp.bfloat16), axis, first).astype(jnp.float32)
    shift = 1
    while shift < length - 1:
        pairs = [(i, i + shift) for i in range(length - shift)]
        s_in = lax.ppermute(s.astype(jnp.bfloat16), axis, pairs).astype(jnp.float32)
        decay = jnp.exp(r)
        if 2 * shift < length - 1:
            r_in = lax.ppermute(r, axis, pairs)
            r = r + r_in
        s = decay[:, None, None] * s_in + s
        shift *= 2
    return s


def slot_table(chosen, capacity, local_experts, n_exp, experts):
    flat = chosen.reshape(-1)
    onehot = (flat[:, None] == jnp.arange(experts, dtype=jnp.int32)[None, :]).astype(jnp.int32)
    preceding_sum = jnp.cumsum(onehot, axis=0) - onehot
    position = jnp.sum(preceding_sum * onehot, axis=1)
    slots = (
        flat % local_experts * (n_exp * capacity)
        + flat // local_experts * capacity
        + position
    )
    return slots.reshape(chosen.shape)


def dispatch_table(slots, total_slots):
    tally = slots[None, :, :] == jnp.arange(total_slots, dtype=jnp.int32)[:, None, None]
    return jnp.any(tally, axis=2).astype(jnp.bfloat16)


def on_device(
    queries,
    keys,
    values,
    log_decay,
    residual,
    out_proj,
    expert_ids,
    route_weights,
    w_gate,
    w_up,
    w_down,
):
    tok = queries.shape[0]
    heads_here = log_decay.shape[1]
    head_dim = queries.shape[1] // heads_here
    q_heads = queries.reshape(tok, heads_here, head_dim)
    k_heads = keys.reshape(tok, heads_here, head_dim)
    v_heads = values.reshape(tok, heads_here, head_dim)
    cum = jnp.cumsum(log_decay, axis=0)
    last = cum[-1]
    scaled_keys = (k_heads.astype(jnp.float32) * jnp.exp(last[None, :] - cum)[:, :, None]).astype(
        jnp.bfloat16
    )
    summary = jnp.einsum("thd,the->hde", scaled_keys, v_heads, preferred_element_type=jnp.float32)
    carried = exclusive_scan(last, summary, "ctx")
    scores = jnp.einsum("thd,shd->hts", q_heads, k_heads, preferred_element_type=jnp.float32)
    place = jnp.arange(tok, dtype=jnp.int32)
    causal = (place[:, None] >= place[None, :])[None]
    diff = cum.T[:, :, None] - cum.T[:, None, :]
    weights = jnp.where(causal, scores * jnp.exp(jnp.where(causal, diff, 0.0)), 0.0).astype(
        jnp.bfloat16
    )
    intra = jnp.einsum("hts,shd->thd", weights, v_heads, preferred_element_type=jnp.float32)
    inter = jnp.exp(cum)[:, :, None] * jnp.einsum(
        "thd,hde->the", q_heads.astype(jnp.float32), carried, precision=lax.Precision.HIGHEST
    )
    attn = intra + inter
    normed = (
        (attn * lax.rsqrt(jnp.mean(attn * attn, axis=-1, keepdims=True) + EPS))
        .astype(jnp.bfloat16)
        .reshape(tok, heads_here * head_dim)
    )
    n_exp = lax.axis_size("exp")
    proj = lax.psum_scatter(
        jnp.dot(normed, out_proj, preferred_element_type=jnp.float32).astype(jnp.bfloat16),
        "exp",
        scatter_dimension=0,
        tiled=True,
    ).astype(jnp.float32)
    feature_vector = residual.astype(jnp.float32) + proj
    moe_in = (
        feature_vector
        * lax.rsqrt(jnp.mean(feature_vector * feature_vector, axis=-1, keepdims=True) + EPS)
    ).astype(jnp.bfloat16)
    local_experts = w_gate.shape[0]
    experts = local_experts * n_exp
    mtok = residual.shape[0]
    width = residual.shape[1]
    capacity = max(2, (5 * mtok + 2 * experts - 1) // (2 * experts))
    total_slots = experts * capacity
    table = slot_table(expert_ids, capacity, local_experts, n_exp, experts)
    packed = jnp.dot(
        dispatch_table(table, total_slots), moe_in, preferred_element_type=jnp.float32
    ).astype(jnp.bfloat16)
    packed = packed.reshape(local_experts, n_exp, capacity, width)
    returned = []
    for e in range(local_experts):
        arrived = lax.all_to_all(packed[e], "exp", split_axis=0, concat_axis=0, tiled=True)
        piece = lax.all_gather(arrived.reshape(n_exp * capacity, width), "ctx", axis=0, tiled=True)
        gate = jnp.dot(piece, w_gate[e], preferred_element_type=jnp.float32)
        upper = jnp.dot(piece, w_up[e], preferred_element_type=jnp.float32)
        acts = (jax.nn.silu(gate) * upper).astype(jnp.bfloat16)
        down = jnp.dot(acts, w_down[e], preferred_element_type=jnp.float32).astype(jnp.bfloat16)
        summed = lax.psum_scatter(down, "ctx", scatter_dimension=0, tiled=True)
        back = lax.all_to_all(
            summed.reshape(n_exp, capacity, width), "exp", split_axis=0, concat_axis=0, tiled=True
        )
        returned.append(back.reshape(n_exp * capacity, width))
    returned = jnp.concatenate(returned, axis=0)
    picker = (
        table.reshape(-1)[:, None] == jnp.arange(total_slots, dtype=jnp.int32)[None, :]
    ).astype(jnp.bfloat16)
    fetched = jnp.dot(picker, returned, preferred_element_type=jnp.float32).reshape(mtok, 2, width)
    moe = route_weights[:, 0:1] * fetched[:, 0] + route_weights[:, 1:2] * fetched[:, 1]
    return (feature_vector + moe).astype(jnp.bfloat16)


def solution(mesh):
    placed = (
        P("ctx", "exp"),
        P("ctx", "exp"),
        P("ctx", "exp"),
        P("ctx", "exp"),
        P(("ctx", "exp"), None),
        P("exp", None),
        P(("ctx", "exp"), None),
        P(("ctx", "exp"), None),
        P("exp", None, "ctx"),
        P("exp", None, "ctx"),
        P("exp", "ctx", None),
    )
    return jax.shard_map(
        on_device, mesh=mesh, in_specs=placed, out_specs=P(("ctx", "exp"), None), check_vma=False
    )
```

```python
import jax
import jax.numpy as jnp
from jax import lax
from jax.sharding import PartitionSpec as P

EPS = 1e-06


def carried_state(last, summary, axis):
    length, here = (lax.axis_size(axis), lax.axis_index(axis))
    heads, hd, _ = summary.shape
    hi = last.astype(jnp.bfloat16)
    lo = (last - hi.astype(jnp.float32)).astype(jnp.bfloat16)
    lane = jnp.arange(hd, dtype=jnp.int32)[None, :]
    rate_row = jnp.where(lane == 0, hi[:, None], jnp.where(lane == 1, lo[:, None], 0.0)).astype(
        jnp.bfloat16
    )
    payload = jnp.concatenate(
        [summary.astype(jnp.bfloat16).reshape(heads, hd * hd), rate_row], axis=1
    )
    everything = lax.all_gather(payload, axis)
    states = everything[:, :, : hd * hd].astype(jnp.float32)
    rates = everything[:, :, hd * hd].astype(jnp.float32) + everything[:, :, hd * hd + 1].astype(
        jnp.float32
    )
    block = jnp.arange(length, dtype=jnp.int32)
    between = ((block[:, None] < block[None, :]) & (block[None, :] < here)).astype(jnp.float32)
    exponent = jnp.sum(between[:, :, None] * rates[None, :, :], axis=1)
    weight = jnp.where((block < here)[:, None], jnp.exp(exponent), 0.0)
    carried = jnp.sum(weight[:, :, None] * states, axis=0)
    return carried.reshape(heads, hd, hd)


def slot_table(chosen_specialist_index, capacity, local_experts, experts):
    flat = chosen_specialist_index.reshape(-1)
    onehot = (flat[:, None] == jnp.arange(experts, dtype=jnp.int32)[None, :]).astype(jnp.int32)
    preceding_sum = jnp.cumsum(onehot, axis=0) - onehot
    position = jnp.sum(preceding_sum * onehot, axis=1)
    slots = (
        flat // local_experts * (capacity * local_experts)
        + position * local_experts
        + flat % local_experts
    )
    return slots.reshape(chosen_specialist_index.shape)


def dispatch_table(slots, total_slots):
    assignment_tally = slots[None, :, :] == jnp.arange(total_slots, dtype=jnp.int32)[:, None, None]
    return jnp.any(assignment_tally, axis=2).astype(jnp.bfloat16)


def on_device(
    queries,
    keys,
    values,
    log_decay,
    residual,
    out_proj,
    expert_ids,
    route_weights,
    w_gate,
    w_up,
    w_down,
):
    tok = queries.shape[0]
    heads_here = log_decay.shape[1]
    head_dim = queries.shape[1] // heads_here
    q_heads = queries.reshape(tok, heads_here, head_dim)
    k_heads = keys.reshape(tok, heads_here, head_dim)
    v_heads = values.reshape(tok, heads_here, head_dim)
    cum = jnp.cumsum(log_decay, axis=0)
    scores = jnp.einsum("thd,shd->hts", q_heads, k_heads, preferred_element_type=jnp.float32)
    place = jnp.arange(tok, dtype=jnp.int32)
    causal = (place[:, None] >= place[None, :])[None]
    diff = cum.T[:, :, None] - cum.T[:, None, :]
    weights = jnp.where(causal, scores * jnp.exp(jnp.where(causal, diff, 0.0)), 0.0).astype(
        jnp.bfloat16
    )
    intra = jnp.einsum("hts,shd->thd", weights, v_heads, preferred_element_type=jnp.float32)
    last = cum[-1]
    scaled_keys = (k_heads.astype(jnp.float32) * jnp.exp(last[None, :] - cum)[:, :, None]).astype(
        jnp.bfloat16
    )
    summary = jnp.einsum("thd,the->hde", scaled_keys, v_heads, preferred_element_type=jnp.float32)
    carried = carried_state(last, summary, "ctx")
    inter = jnp.exp(cum)[:, :, None] * jnp.einsum(
        "thd,hde->the", q_heads.astype(jnp.float32), carried, precision=lax.Precision.HIGHEST
    )
    attn = intra + inter
    normed = (
        (attn * lax.rsqrt(jnp.mean(attn * attn, axis=-1, keepdims=True) + EPS))
        .astype(jnp.bfloat16)
        .reshape(tok, heads_here * head_dim)
    )
    n_exp = lax.axis_size("exp")
    proj = lax.psum_scatter(
        jnp.dot(normed, out_proj, preferred_element_type=jnp.float32).astype(jnp.bfloat16),
        "exp",
        scatter_dimension=0,
        tiled=True,
    ).astype(jnp.float32)
    feature_vector = residual.astype(jnp.float32) + proj
    moe_in = (
        feature_vector
        * lax.rsqrt(jnp.mean(feature_vector * feature_vector, axis=-1, keepdims=True) + EPS)
    ).astype(jnp.bfloat16)
    local_experts = w_gate.shape[0]
    experts = local_experts * n_exp
    mtok = residual.shape[0]
    width = residual.shape[1]
    capacity = max(2, (5 * mtok + 2 * experts - 1) // (2 * experts))
    total_slots = experts * capacity
    local_slot_table = slot_table(expert_ids, capacity, local_experts, experts)
    packed = jnp.dot(
        dispatch_table(local_slot_table, total_slots), moe_in, preferred_element_type=jnp.float32
    ).astype(jnp.bfloat16)
    packed = packed.reshape(n_exp, capacity, local_experts, width)
    arrived = lax.all_to_all(packed, "exp", split_axis=0, concat_axis=1, tiled=True).reshape(
        n_exp * capacity, local_experts, width
    )
    piece = lax.all_gather(arrived, "ctx", axis=0, tiled=True)
    gate = jnp.einsum("red,edf->ref", piece, w_gate, preferred_element_type=jnp.float32)
    upper = jnp.einsum("red,edf->ref", piece, w_up, preferred_element_type=jnp.float32)
    acts = (jax.nn.silu(gate) * upper).astype(jnp.bfloat16)
    summed = lax.psum_scatter(
        jnp.einsum("ref,efd->red", acts, w_down, preferred_element_type=jnp.float32).astype(
            jnp.bfloat16
        ),
        "ctx",
        scatter_dimension=0,
        tiled=True,
    )
    outgoing = summed.reshape(n_exp, capacity, local_experts, width)
    returned = lax.all_to_all(outgoing, "exp", split_axis=0, concat_axis=0, tiled=True).reshape(
        total_slots, width
    )
    picker = (
        local_slot_table.reshape(-1)[:, None] == jnp.arange(total_slots, dtype=jnp.int32)[None, :]
    ).astype(jnp.bfloat16)
    fetched = jnp.dot(picker, returned, preferred_element_type=jnp.float32).reshape(mtok, 2, width)
    moe = route_weights[:, 0:1] * fetched[:, 0] + route_weights[:, 1:2] * fetched[:, 1]
    return (feature_vector + moe).astype(jnp.bfloat16)


def solution(mesh):
    placed = (
        P("ctx", "exp"),
        P("ctx", "exp"),
        P("ctx", "exp"),
        P("ctx", "exp"),
        P(("ctx", "exp"), None),
        P("exp", None),
        P(("ctx", "exp"), None),
        P(("ctx", "exp"), None),
        P("exp", None, "ctx"),
        P("exp", None, "ctx"),
        P("exp", "ctx", None),
    )
    return jax.shard_map(
        on_device, mesh=mesh, in_specs=placed, out_specs=P(("ctx", "exp"), None), check_vma=False
    )
```

```python
import jax
import jax.numpy as jnp
from jax import lax
from jax.sharding import PartitionSpec as P

EPS = 1e-06


def carried_state(last, summary, axis):
    length, here = (lax.axis_size(axis), lax.axis_index(axis))
    heads, hd, _ = summary.shape
    hi = last.astype(jnp.bfloat16)
    lo = (last - hi.astype(jnp.float32)).astype(jnp.bfloat16)
    lane = jnp.arange(hd, dtype=jnp.int32)[None, :]
    rate_row = jnp.where(lane == 0, hi[:, None], jnp.where(lane == 1, lo[:, None], 0.0)).astype(
        jnp.bfloat16
    )
    payload = jnp.concatenate(
        [summary.astype(jnp.bfloat16).reshape(heads, hd * hd), rate_row], axis=1
    )
    everything = lax.all_to_all(
        jnp.broadcast_to(payload[None], (length,) + payload.shape), axis, 0, 0, tiled=True
    )
    states = everything[:, :, : hd * hd].astype(jnp.float32)
    rates = everything[:, :, hd * hd].astype(jnp.float32) + everything[:, :, hd * hd + 1].astype(
        jnp.float32
    )
    block = jnp.arange(length, dtype=jnp.int32)
    between = ((block[:, None] < block[None, :]) & (block[None, :] < here)).astype(jnp.float32)
    exponent = jnp.sum(between[:, :, None] * rates[None, :, :], axis=1)
    weight = jnp.where((block < here)[:, None], jnp.exp(exponent), 0.0)
    carried = jnp.sum(weight[:, :, None] * states, axis=0)
    return carried.reshape(heads, hd, hd)


def slot_table(chosen_specialist_index, capacity, local_experts, experts):
    flat = chosen_specialist_index.reshape(-1)
    onehot = (flat[:, None] == jnp.arange(experts, dtype=jnp.int32)[None, :]).astype(jnp.int32)
    preceding_sum = jnp.cumsum(onehot, axis=0) - onehot
    position = jnp.sum(preceding_sum * onehot, axis=1)
    slots = (
        flat // local_experts * (capacity * local_experts)
        + position * local_experts
        + flat % local_experts
    )
    return slots.reshape(chosen_specialist_index.shape)


def dispatch_table(slots, total_slots):
    assignment_tally = slots[None, :, :] == jnp.arange(total_slots, dtype=jnp.int32)[:, None, None]
    return jnp.any(assignment_tally, axis=2).astype(jnp.bfloat16)


def on_device(
    queries,
    keys,
    values,
    log_decay,
    residual,
    out_proj,
    expert_ids,
    route_weights,
    w_gate,
    w_up,
    w_down,
):
    tok = queries.shape[0]
    heads_here = log_decay.shape[1]
    head_dim = queries.shape[1] // heads_here
    q_heads = queries.reshape(tok, heads_here, head_dim)
    k_heads = keys.reshape(tok, heads_here, head_dim)
    v_heads = values.reshape(tok, heads_here, head_dim)
    cum = jnp.cumsum(log_decay, axis=0)
    scores = jnp.einsum("thd,shd->hts", q_heads, k_heads, preferred_element_type=jnp.float32)
    place = jnp.arange(tok, dtype=jnp.int32)
    causal = (place[:, None] >= place[None, :])[None]
    diff = cum.T[:, :, None] - cum.T[:, None, :]
    weights = jnp.where(causal, scores * jnp.exp(jnp.where(causal, diff, 0.0)), 0.0).astype(
        jnp.bfloat16
    )
    intra = jnp.einsum("hts,shd->thd", weights, v_heads, preferred_element_type=jnp.float32)
    last = cum[-1]
    scaled_keys = (k_heads.astype(jnp.float32) * jnp.exp(last[None, :] - cum)[:, :, None]).astype(
        jnp.bfloat16
    )
    summary = jnp.einsum("thd,the->hde", scaled_keys, v_heads, preferred_element_type=jnp.float32)
    carried = carried_state(last, summary, "ctx")
    inter = jnp.exp(cum)[:, :, None] * jnp.einsum(
        "thd,hde->the", q_heads.astype(jnp.float32), carried, precision=lax.Precision.HIGHEST
    )
    attn = intra + inter
    normed = (
        (attn * lax.rsqrt(jnp.mean(attn * attn, axis=-1, keepdims=True) + EPS))
        .astype(jnp.bfloat16)
        .reshape(tok, heads_here * head_dim)
    )
    n_exp = lax.axis_size("exp")
    proj = lax.psum_scatter(
        jnp.dot(normed, out_proj, preferred_element_type=jnp.float32).astype(jnp.bfloat16),
        "exp",
        scatter_dimension=0,
        tiled=True,
    ).astype(jnp.float32)
    feature_vector = residual.astype(jnp.float32) + proj
    moe_in = (
        feature_vector
        * lax.rsqrt(jnp.mean(feature_vector * feature_vector, axis=-1, keepdims=True) + EPS)
    ).astype(jnp.bfloat16)
    local_experts = w_gate.shape[0]
    experts = local_experts * n_exp
    mtok = residual.shape[0]
    width = residual.shape[1]
    capacity = max(2, (5 * mtok + 2 * experts - 1) // (2 * experts))
    total_slots = experts * capacity
    local_slot_table = slot_table(expert_ids, capacity, local_experts, experts)
    packed = jnp.dot(
        dispatch_table(local_slot_table, total_slots), moe_in, preferred_element_type=jnp.float32
    ).astype(jnp.bfloat16)
    packed = packed.reshape(n_exp, capacity, local_experts, width)
    arrived = lax.all_to_all(packed, "exp", split_axis=0, concat_axis=1, tiled=True).reshape(
        n_exp * capacity, local_experts, width
    )
    piece = lax.all_gather(arrived, "ctx", axis=0, tiled=True)
    gate = jnp.einsum("red,edf->ref", piece, w_gate, preferred_element_type=jnp.float32)
    upper = jnp.einsum("red,edf->ref", piece, w_up, preferred_element_type=jnp.float32)
    acts = (jax.nn.silu(gate) * upper).astype(jnp.bfloat16)
    summed = lax.psum_scatter(
        jnp.einsum("ref,efd->red", acts, w_down, preferred_element_type=jnp.float32).astype(
            jnp.bfloat16
        ),
        "ctx",
        scatter_dimension=0,
        tiled=True,
    )
    outgoing = summed.reshape(n_exp, capacity, local_experts, width)
    returned = lax.all_to_all(outgoing, "exp", split_axis=0, concat_axis=0, tiled=True).reshape(
        total_slots, width
    )
    picker = (
        local_slot_table.reshape(-1)[:, None] == jnp.arange(total_slots, dtype=jnp.int32)[None, :]
    ).astype(jnp.bfloat16)
    fetched = jnp.dot(picker, returned, preferred_element_type=jnp.float32).reshape(mtok, 2, width)
    moe = route_weights[:, 0:1] * fetched[:, 0] + route_weights[:, 1:2] * fetched[:, 1]
    return (feature_vector + moe).astype(jnp.bfloat16)


def solution(mesh):
    placed = (
        P("ctx", "exp"),
        P("ctx", "exp"),
        P("ctx", "exp"),
        P("ctx", "exp"),
        P(("ctx", "exp"), None),
        P("exp", None),
        P(("ctx", "exp"), None),
        P(("ctx", "exp"), None),
        P("exp", None, "ctx"),
        P("exp", None, "ctx"),
        P("exp", "ctx", None),
    )
    return jax.shard_map(
        on_device, mesh=mesh, in_specs=placed, out_specs=P(("ctx", "exp"), None), check_vma=False
    )
```

```python
import jax
import jax.numpy as jnp
from jax import lax
from jax.sharding import PartitionSpec as P

EPS = 1e-06


def carried_state(last, summary, axis):
    length, here = (lax.axis_size(axis), lax.axis_index(axis))
    heads, hd, _ = summary.shape
    hi = last.astype(jnp.bfloat16)
    lo = (last - hi.astype(jnp.float32)).astype(jnp.bfloat16)
    lane = jnp.arange(hd, dtype=jnp.int32)[None, :]
    rate_row = jnp.where(lane == 0, hi[:, None], jnp.where(lane == 1, lo[:, None], 0.0)).astype(
        jnp.bfloat16
    )
    payload = jnp.concatenate(
        [summary.astype(jnp.bfloat16).reshape(heads, hd * hd), rate_row], axis=1
    )
    everything = lax.all_gather(payload, axis)
    states = everything[:, :, : hd * hd].astype(jnp.float32)
    rates = everything[:, :, hd * hd].astype(jnp.float32) + everything[:, :, hd * hd + 1].astype(
        jnp.float32
    )
    block = jnp.arange(length, dtype=jnp.int32)
    between = ((block[:, None] < block[None, :]) & (block[None, :] < here)).astype(jnp.float32)
    exponent = jnp.sum(between[:, :, None] * rates[None, :, :], axis=1)
    weight = jnp.where((block < here)[:, None], jnp.exp(exponent), 0.0)
    carried = jnp.sum(weight[:, :, None] * states, axis=0)
    return carried.reshape(heads, hd, hd)


def slot_table(chosen_specialist_index, capacity, local_experts, experts):
    flat = chosen_specialist_index.reshape(-1)
    onehot = (flat[:, None] == jnp.arange(experts, dtype=jnp.int32)[None, :]).astype(jnp.int32)
    preceding_sum = jnp.cumsum(onehot, axis=0) - onehot
    position = jnp.sum(preceding_sum * onehot, axis=1)
    slots = (
        flat // local_experts * (capacity * local_experts)
        + position * local_experts
        + flat % local_experts
    )
    return slots.reshape(chosen_specialist_index.shape)


def dispatch_table(slots, total_slots):
    assignment_tally = slots[None, :, :] == jnp.arange(total_slots, dtype=jnp.int32)[:, None, None]
    return jnp.any(assignment_tally, axis=2).astype(jnp.bfloat16)


def on_device(
    queries,
    keys,
    values,
    log_decay,
    residual,
    out_proj,
    expert_ids,
    route_weights,
    w_gate,
    w_up,
    w_down,
):
    tok = queries.shape[0]
    heads_here = log_decay.shape[1]
    head_dim = queries.shape[1] // heads_here
    q_heads = queries.reshape(tok, heads_here, head_dim)
    k_heads = keys.reshape(tok, heads_here, head_dim)
    v_heads = values.reshape(tok, heads_here, head_dim)
    cum = jnp.cumsum(log_decay, axis=0)
    scores = jnp.einsum("thd,shd->hts", q_heads, k_heads, preferred_element_type=jnp.float32)
    place = jnp.arange(tok, dtype=jnp.int32)
    causal = (place[:, None] >= place[None, :])[None]
    diff = cum.T[:, :, None] - cum.T[:, None, :]
    weights = jnp.where(causal, scores * jnp.exp(jnp.where(causal, diff, 0.0)), 0.0).astype(
        jnp.bfloat16
    )
    intra = jnp.einsum("hts,shd->thd", weights, v_heads, preferred_element_type=jnp.float32)
    last = cum[-1]
    scaled_keys = (k_heads.astype(jnp.float32) * jnp.exp(last[None, :] - cum)[:, :, None]).astype(
        jnp.bfloat16
    )
    summary = jnp.einsum("thd,the->hde", scaled_keys, v_heads, preferred_element_type=jnp.float32)
    carried = carried_state(last, summary, "ctx")
    inter = jnp.exp(cum)[:, :, None] * jnp.einsum(
        "thd,hde->the", q_heads.astype(jnp.float32), carried, precision=lax.Precision.HIGHEST
    )
    attn = intra + inter
    normed = (
        (attn * lax.rsqrt(jnp.mean(attn * attn, axis=-1, keepdims=True) + EPS))
        .astype(jnp.bfloat16)
        .reshape(tok, heads_here * head_dim)
    )
    n_exp = lax.axis_size("exp")
    proj = lax.psum_scatter(
        jnp.dot(normed, out_proj, preferred_element_type=jnp.float32).astype(jnp.bfloat16),
        "exp",
        scatter_dimension=0,
        tiled=True,
    ).astype(jnp.float32)
    feature_vector = residual.astype(jnp.float32) + proj
    moe_in = (
        feature_vector
        * lax.rsqrt(jnp.mean(feature_vector * feature_vector, axis=-1, keepdims=True) + EPS)
    ).astype(jnp.bfloat16)
    local_experts = w_gate.shape[0]
    experts = local_experts * n_exp
    mtok = residual.shape[0]
    width = residual.shape[1]
    capacity = max(2, (5 * mtok + 2 * experts - 1) // (2 * experts))
    total_slots = experts * capacity
    local_slot_table = slot_table(expert_ids, capacity, local_experts, experts)
    packed = jnp.dot(
        dispatch_table(local_slot_table, total_slots), moe_in, preferred_element_type=jnp.float32
    ).astype(jnp.bfloat16)
    packed = packed.reshape(n_exp, capacity, local_experts, width)
    arrived = lax.all_to_all(packed, "exp", split_axis=0, concat_axis=1, tiled=True).reshape(
        n_exp * capacity, local_experts, width
    )
    piece = lax.all_gather(arrived, "ctx", axis=0, tiled=True)
    hidden_units = w_gate.shape[2]
    both = jnp.einsum(
        "red,edf->ref",
        piece,
        jnp.concatenate([w_gate, w_up], axis=2),
        preferred_element_type=jnp.float32,
    )
    gate = both[:, :, :hidden_units]
    upper = both[:, :, hidden_units:]
    acts = (jax.nn.silu(gate) * upper).astype(jnp.bfloat16)
    summed = lax.psum_scatter(
        jnp.einsum("ref,efd->red", acts, w_down, preferred_element_type=jnp.float32).astype(
            jnp.bfloat16
        ),
        "ctx",
        scatter_dimension=0,
        tiled=True,
    )
    outgoing = summed.reshape(n_exp, capacity, local_experts, width)
    returned = lax.all_to_all(outgoing, "exp", split_axis=0, concat_axis=0, tiled=True).reshape(
        total_slots, width
    )
    picker = (
        local_slot_table.reshape(-1)[:, None] == jnp.arange(total_slots, dtype=jnp.int32)[None, :]
    ).astype(jnp.bfloat16)
    fetched = jnp.dot(picker, returned, preferred_element_type=jnp.float32).reshape(mtok, 2, width)
    moe = route_weights[:, 0:1] * fetched[:, 0] + route_weights[:, 1:2] * fetched[:, 1]
    return (feature_vector + moe).astype(jnp.bfloat16)


def solution(mesh):
    placed = (
        P("ctx", "exp"),
        P("ctx", "exp"),
        P("ctx", "exp"),
        P("ctx", "exp"),
        P(("ctx", "exp"), None),
        P("exp", None),
        P(("ctx", "exp"), None),
        P(("ctx", "exp"), None),
        P("exp", None, "ctx"),
        P("exp", None, "ctx"),
        P("exp", "ctx", None),
    )
    return jax.shard_map(
        on_device, mesh=mesh, in_specs=placed, out_specs=P(("ctx", "exp"), None), check_vma=False
    )
```

```python
import jax
import jax.numpy as jnp
from jax import lax
from jax.sharding import PartitionSpec as P

EPS = 1e-06


def carried_state(last, summary, axis):
    length, here = (lax.axis_size(axis), lax.axis_index(axis))
    heads, hd, _ = summary.shape
    hi = last.astype(jnp.bfloat16)
    lo = (last - hi.astype(jnp.float32)).astype(jnp.bfloat16)
    lane = jnp.arange(hd, dtype=jnp.int32)[None, :]
    rate_row = jnp.where(lane == 0, hi[:, None], jnp.where(lane == 1, lo[:, None], 0.0)).astype(
        jnp.bfloat16
    )
    payload = jnp.concatenate(
        [summary.astype(jnp.bfloat16).reshape(heads, hd * hd), rate_row], axis=1
    )
    everything = lax.all_gather(payload, axis)
    states = everything[:, :, : hd * hd].astype(jnp.float32)
    rates = everything[:, :, hd * hd].astype(jnp.float32) + everything[:, :, hd * hd + 1].astype(
        jnp.float32
    )
    block = jnp.arange(length, dtype=jnp.int32)
    between = ((block[:, None] < block[None, :]) & (block[None, :] < here)).astype(jnp.float32)
    exponent = jnp.sum(between[:, :, None] * rates[None, :, :], axis=1)
    weight = jnp.where((block < here)[:, None], jnp.exp(exponent), 0.0)
    carried = jnp.einsum("kh,khx->hx", weight, states, precision=lax.Precision.HIGHEST)
    return carried.reshape(heads, hd, hd)


def slot_table(chosen_specialist_index, capacity, local_experts, experts):
    flat = chosen_specialist_index.reshape(-1)
    onehot = (flat[:, None] == jnp.arange(experts, dtype=jnp.int32)[None, :]).astype(jnp.int32)
    preceding_sum = jnp.cumsum(onehot, axis=0) - onehot
    position = jnp.sum(preceding_sum * onehot, axis=1)
    slots = (
        flat // local_experts * (capacity * local_experts)
        + position * local_experts
        + flat % local_experts
    )
    return slots.reshape(chosen_specialist_index.shape)


def dispatch_table(slots, total_slots):
    assignment_tally = slots[None, :, :] == jnp.arange(total_slots, dtype=jnp.int32)[:, None, None]
    return jnp.any(assignment_tally, axis=2).astype(jnp.bfloat16)


def on_device(
    queries,
    keys,
    values,
    log_decay,
    residual,
    out_proj,
    expert_ids,
    route_weights,
    w_gate,
    w_up,
    w_down,
):
    tok = queries.shape[0]
    heads_here = log_decay.shape[1]
    head_dim = queries.shape[1] // heads_here
    q_heads = queries.reshape(tok, heads_here, head_dim)
    k_heads = keys.reshape(tok, heads_here, head_dim)
    v_heads = values.reshape(tok, heads_here, head_dim)
    place = jnp.arange(tok, dtype=jnp.int32)
    lower = (place[:, None] >= place[None, :]).astype(jnp.float32)
    cum = jnp.dot(lower, log_decay, precision=lax.Precision.HIGHEST)
    scores = jnp.einsum("thd,shd->hts", q_heads, k_heads, preferred_element_type=jnp.float32)
    causal = (place[:, None] >= place[None, :])[None]
    diff = cum.T[:, :, None] - cum.T[:, None, :]
    weights = jnp.where(causal, scores * jnp.exp(jnp.where(causal, diff, 0.0)), 0.0).astype(
        jnp.bfloat16
    )
    intra = jnp.einsum("hts,shd->thd", weights, v_heads, preferred_element_type=jnp.float32)
    last = cum[-1]
    scaled_keys = (k_heads.astype(jnp.float32) * jnp.exp(last[None, :] - cum)[:, :, None]).astype(
        jnp.bfloat16
    )
    summary = jnp.einsum("thd,the->hde", scaled_keys, v_heads, preferred_element_type=jnp.float32)
    carried = carried_state(last, summary, "ctx")
    inter = jnp.exp(cum)[:, :, None] * jnp.einsum(
        "thd,hde->the", q_heads.astype(jnp.float32), carried, precision=lax.Precision.HIGHEST
    )
    attn = intra + inter
    normed = (
        (attn * lax.rsqrt(jnp.mean(attn * attn, axis=-1, keepdims=True) + EPS))
        .astype(jnp.bfloat16)
        .reshape(tok, heads_here * head_dim)
    )
    n_exp = lax.axis_size("exp")
    proj = lax.psum_scatter(
        jnp.dot(normed, out_proj, preferred_element_type=jnp.float32).astype(jnp.bfloat16),
        "exp",
        scatter_dimension=0,
        tiled=True,
    ).astype(jnp.float32)
    feature_vector = residual.astype(jnp.float32) + proj
    moe_in = (
        feature_vector
        * lax.rsqrt(jnp.mean(feature_vector * feature_vector, axis=-1, keepdims=True) + EPS)
    ).astype(jnp.bfloat16)
    local_experts = w_gate.shape[0]
    experts = local_experts * n_exp
    mtok = residual.shape[0]
    width = residual.shape[1]
    capacity = max(2, (5 * mtok + 2 * experts - 1) // (2 * experts))
    total_slots = experts * capacity
    local_slot_table = slot_table(expert_ids, capacity, local_experts, experts)
    packed = jnp.dot(
        dispatch_table(local_slot_table, total_slots), moe_in, preferred_element_type=jnp.float32
    ).astype(jnp.bfloat16)
    packed = packed.reshape(n_exp, capacity, local_experts, width)
    arrived = lax.all_to_all(packed, "exp", split_axis=0, concat_axis=1, tiled=True).reshape(
        n_exp * capacity, local_experts, width
    )
    piece = lax.all_gather(arrived, "ctx", axis=0, tiled=True)
    hidden_units = w_gate.shape[2]
    both = jnp.einsum(
        "red,edf->ref",
        piece,
        jnp.concatenate([w_gate, w_up], axis=2),
        preferred_element_type=jnp.float32,
    )
    gate = both[:, :, :hidden_units]
    upper = both[:, :, hidden_units:]
    acts = (jax.nn.silu(gate) * upper).astype(jnp.bfloat16)
    summed = lax.psum_scatter(
        jnp.einsum("ref,efd->red", acts, w_down, preferred_element_type=jnp.float32).astype(
            jnp.bfloat16
        ),
        "ctx",
        scatter_dimension=0,
        tiled=True,
    )
    outgoing = summed.reshape(n_exp, capacity, local_experts, width)
    returned = lax.all_to_all(outgoing, "exp", split_axis=0, concat_axis=0, tiled=True).reshape(
        total_slots, width
    )
    picker = (
        local_slot_table.reshape(-1)[:, None] == jnp.arange(total_slots, dtype=jnp.int32)[None, :]
    ).astype(jnp.bfloat16)
    fetched = jnp.dot(picker, returned, preferred_element_type=jnp.float32).reshape(mtok, 2, width)
    moe = route_weights[:, 0:1] * fetched[:, 0] + route_weights[:, 1:2] * fetched[:, 1]
    return (feature_vector + moe).astype(jnp.bfloat16)


def solution(mesh):
    placed = (
        P("ctx", "exp"),
        P("ctx", "exp"),
        P("ctx", "exp"),
        P("ctx", "exp"),
        P(("ctx", "exp"), None),
        P("exp", None),
        P(("ctx", "exp"), None),
        P(("ctx", "exp"), None),
        P("exp", None, "ctx"),
        P("exp", None, "ctx"),
        P("exp", "ctx", None),
    )
    return jax.shard_map(
        on_device, mesh=mesh, in_specs=placed, out_specs=P(("ctx", "exp"), None), check_vma=False
    )
```

```python
import jax
import jax.numpy as jnp
from jax import lax
from jax.sharding import PartitionSpec as P

EPS = 1e-06


def pack(rate, state):
    heads, hd, _ = state.shape
    hi = rate.astype(jnp.bfloat16)
    lo = (rate - hi.astype(jnp.float32)).astype(jnp.bfloat16)
    lane = jnp.arange(hd, dtype=jnp.int32)[None, :]
    rate_row = jnp.where(lane == 0, hi[:, None], jnp.where(lane == 1, lo[:, None], 0.0)).astype(
        jnp.bfloat16
    )
    return jnp.concatenate([state.astype(jnp.bfloat16).reshape(heads, hd * hd), rate_row], axis=1)


def unpack(payload, hd):
    heads = payload.shape[0]
    state = payload[:, : hd * hd].astype(jnp.float32).reshape(heads, hd, hd)
    rate = payload[:, hd * hd].astype(jnp.float32) + payload[:, hd * hd + 1].astype(jnp.float32)
    return rate, state


def carried_state(last, summary, axis):
    length = lax.axis_size(axis)
    hd = summary.shape[1]
    incl_r, incl_s = last, summary
    excl_r, excl_s = jnp.zeros_like(last), jnp.zeros_like(summary)
    shift = 1
    while shift < length:
        pairs = [(i, i + shift) for i in range(length - shift)]
        in_r, in_s = unpack(lax.ppermute(pack(incl_r, incl_s), axis, pairs), hd)
        excl_s = jnp.exp(excl_r)[:, None, None] * in_s + excl_s
        excl_r = in_r + excl_r
        if 2 * shift < length:
            incl_s = jnp.exp(incl_r)[:, None, None] * in_s + incl_s
            incl_r = in_r + incl_r
        shift *= 2
    return excl_s


def slot_table(chosen_specialist_index, capacity, local_experts, experts):
    flat = chosen_specialist_index.reshape(-1)
    onehot = (flat[:, None] == jnp.arange(experts, dtype=jnp.int32)[None, :]).astype(jnp.int32)
    preceding_sum = jnp.cumsum(onehot, axis=0) - onehot
    position = jnp.sum(preceding_sum * onehot, axis=1)
    slots = (
        flat // local_experts * (capacity * local_experts)
        + position * local_experts
        + flat % local_experts
    )
    return slots.reshape(chosen_specialist_index.shape)


def dispatch_table(slots, total_slots):
    assignment_tally = slots[None, :, :] == jnp.arange(total_slots, dtype=jnp.int32)[:, None, None]
    return jnp.any(assignment_tally, axis=2).astype(jnp.bfloat16)


def on_device(
    queries,
    keys,
    values,
    log_decay,
    residual,
    out_proj,
    expert_ids,
    route_weights,
    w_gate,
    w_up,
    w_down,
):
    tok = queries.shape[0]
    heads_here = log_decay.shape[1]
    head_dim = queries.shape[1] // heads_here
    q_heads = queries.reshape(tok, heads_here, head_dim)
    k_heads = keys.reshape(tok, heads_here, head_dim)
    v_heads = values.reshape(tok, heads_here, head_dim)
    place = jnp.arange(tok, dtype=jnp.int32)
    lower = (place[:, None] >= place[None, :]).astype(jnp.float32)
    cum = jnp.dot(lower, log_decay, precision=lax.Precision.HIGHEST)
    scores = jnp.einsum("thd,shd->hts", q_heads, k_heads, preferred_element_type=jnp.float32)
    causal = (place[:, None] >= place[None, :])[None]
    diff = cum.T[:, :, None] - cum.T[:, None, :]
    weights = jnp.where(causal, scores * jnp.exp(jnp.where(causal, diff, 0.0)), 0.0).astype(
        jnp.bfloat16
    )
    intra = jnp.einsum("hts,shd->thd", weights, v_heads, preferred_element_type=jnp.float32)
    last = cum[-1]
    scaled_keys = (k_heads.astype(jnp.float32) * jnp.exp(last[None, :] - cum)[:, :, None]).astype(
        jnp.bfloat16
    )
    summary = jnp.einsum("thd,the->hde", scaled_keys, v_heads, preferred_element_type=jnp.float32)
    carried = carried_state(last, summary, "ctx")
    inter = jnp.exp(cum)[:, :, None] * jnp.einsum(
        "thd,hde->the", q_heads.astype(jnp.float32), carried, precision=lax.Precision.HIGHEST
    )
    attn = intra + inter
    normed = (
        (attn * lax.rsqrt(jnp.mean(attn * attn, axis=-1, keepdims=True) + EPS))
        .astype(jnp.bfloat16)
        .reshape(tok, heads_here * head_dim)
    )
    n_exp = lax.axis_size("exp")
    proj = lax.psum_scatter(
        jnp.dot(normed, out_proj, preferred_element_type=jnp.float32).astype(jnp.bfloat16),
        "exp",
        scatter_dimension=0,
        tiled=True,
    ).astype(jnp.float32)
    feature_vector = residual.astype(jnp.float32) + proj
    moe_in = (
        feature_vector
        * lax.rsqrt(jnp.mean(feature_vector * feature_vector, axis=-1, keepdims=True) + EPS)
    ).astype(jnp.bfloat16)
    local_experts = w_gate.shape[0]
    experts = local_experts * n_exp
    mtok = residual.shape[0]
    width = residual.shape[1]
    capacity = max(2, (5 * mtok + 2 * experts - 1) // (2 * experts))
    total_slots = experts * capacity
    local_slot_table = slot_table(expert_ids, capacity, local_experts, experts)
    packed = jnp.dot(
        dispatch_table(local_slot_table, total_slots), moe_in, preferred_element_type=jnp.float32
    ).astype(jnp.bfloat16)
    packed = packed.reshape(n_exp, capacity, local_experts, width)
    arrived = lax.all_to_all(packed, "exp", split_axis=0, concat_axis=1, tiled=True).reshape(
        n_exp * capacity, local_experts, width
    )
    piece = lax.all_gather(arrived, "ctx", axis=0, tiled=True)
    hidden_units = w_gate.shape[2]
    both = jnp.einsum(
        "red,edf->ref",
        piece,
        jnp.concatenate([w_gate, w_up], axis=2),
        preferred_element_type=jnp.float32,
    )
    gate = both[:, :, :hidden_units]
    upper = both[:, :, hidden_units:]
    acts = (jax.nn.silu(gate) * upper).astype(jnp.bfloat16)
    summed = lax.psum_scatter(
        jnp.einsum("ref,efd->red", acts, w_down, preferred_element_type=jnp.float32).astype(
            jnp.bfloat16
        ),
        "ctx",
        scatter_dimension=0,
        tiled=True,
    )
    outgoing = summed.reshape(n_exp, capacity, local_experts, width)
    returned = lax.all_to_all(outgoing, "exp", split_axis=0, concat_axis=0, tiled=True).reshape(
        total_slots, width
    )
    picker = (
        local_slot_table.reshape(-1)[:, None] == jnp.arange(total_slots, dtype=jnp.int32)[None, :]
    ).astype(jnp.bfloat16)
    fetched = jnp.dot(picker, returned, preferred_element_type=jnp.float32).reshape(mtok, 2, width)
    moe = route_weights[:, 0:1] * fetched[:, 0] + route_weights[:, 1:2] * fetched[:, 1]
    return (feature_vector + moe).astype(jnp.bfloat16)


def solution(mesh):
    placed = (
        P("ctx", "exp"),
        P("ctx", "exp"),
        P("ctx", "exp"),
        P("ctx", "exp"),
        P(("ctx", "exp"), None),
        P("exp", None),
        P(("ctx", "exp"), None),
        P(("ctx", "exp"), None),
        P("exp", None, "ctx"),
        P("exp", None, "ctx"),
        P("exp", "ctx", None),
    )
    return jax.shard_map(
        on_device, mesh=mesh, in_specs=placed, out_specs=P(("ctx", "exp"), None), check_vma=False
    )
```

```python
import jax
import jax.numpy as jnp
from jax import lax
from jax.sharding import PartitionSpec as P

EPS = 1e-06


def pack(rate, state):
    heads, hd, _ = state.shape
    hi = rate.astype(jnp.bfloat16)
    lo = (rate - hi.astype(jnp.float32)).astype(jnp.bfloat16)
    lane = jnp.arange(hd, dtype=jnp.int32)[None, :]
    rate_row = jnp.where(lane == 0, hi[:, None], jnp.where(lane == 1, lo[:, None], 0.0)).astype(
        jnp.bfloat16
    )
    return jnp.concatenate([state.astype(jnp.bfloat16).reshape(heads, hd * hd), rate_row], axis=1)


def unpack(payload, hd):
    heads = payload.shape[0]
    state = payload[:, : hd * hd].astype(jnp.float32).reshape(heads, hd, hd)
    rate = payload[:, hd * hd].astype(jnp.float32) + payload[:, hd * hd + 1].astype(jnp.float32)
    return rate, state


def combine(earlier, later):
    return (earlier[0] + later[0], jnp.exp(later[0])[:, None, None] * earlier[1] + later[1])


def carried_state(last, summary, axis):
    length = lax.axis_size(axis)
    hd = summary.shape[1]
    incl = (last, summary)
    excl = (jnp.zeros_like(last), jnp.zeros_like(summary))
    shift = 1
    while shift < length:
        sent = pack(*incl)
        arrived = []
        for k in range(1, 4):
            if k * shift < length:
                pairs = [(i, i + k * shift) for i in range(length - k * shift)]
                arrived.append(unpack(lax.ppermute(sent, axis, pairs), hd))
        before = arrived[-1]
        for part in reversed(arrived[:-1]):
            before = combine(before, part)
        excl = combine(before, excl)
        if 4 * shift < length:
            incl = combine(before, incl)
        shift *= 4
    return excl[1]


def slot_table(chosen_specialist_index, capacity, local_experts, experts):
    flat = chosen_specialist_index.reshape(-1)
    onehot = (flat[:, None] == jnp.arange(experts, dtype=jnp.int32)[None, :]).astype(jnp.int32)
    preceding_sum = jnp.cumsum(onehot, axis=0) - onehot
    position = jnp.sum(preceding_sum * onehot, axis=1)
    slots = (
        flat // local_experts * (capacity * local_experts)
        + position * local_experts
        + flat % local_experts
    )
    return slots.reshape(chosen_specialist_index.shape)


def dispatch_table(slots, total_slots):
    assignment_tally = slots[None, :, :] == jnp.arange(total_slots, dtype=jnp.int32)[:, None, None]
    return jnp.any(assignment_tally, axis=2).astype(jnp.bfloat16)


def on_device(
    queries,
    keys,
    values,
    log_decay,
    residual,
    out_proj,
    expert_ids,
    route_weights,
    w_gate,
    w_up,
    w_down,
):
    tok = queries.shape[0]
    heads_here = log_decay.shape[1]
    head_dim = queries.shape[1] // heads_here
    q_heads = queries.reshape(tok, heads_here, head_dim)
    k_heads = keys.reshape(tok, heads_here, head_dim)
    v_heads = values.reshape(tok, heads_here, head_dim)
    place = jnp.arange(tok, dtype=jnp.int32)
    lower = (place[:, None] >= place[None, :]).astype(jnp.float32)
    cum = jnp.dot(lower, log_decay, precision=lax.Precision.HIGHEST)
    scores = jnp.einsum("thd,shd->hts", q_heads, k_heads, preferred_element_type=jnp.float32)
    causal = (place[:, None] >= place[None, :])[None]
    diff = cum.T[:, :, None] - cum.T[:, None, :]
    weights = jnp.where(causal, scores * jnp.exp(jnp.where(causal, diff, 0.0)), 0.0).astype(
        jnp.bfloat16
    )
    intra = jnp.einsum("hts,shd->thd", weights, v_heads, preferred_element_type=jnp.float32)
    last = cum[-1]
    scaled_keys = (k_heads.astype(jnp.float32) * jnp.exp(last[None, :] - cum)[:, :, None]).astype(
        jnp.bfloat16
    )
    summary = jnp.einsum("thd,the->hde", scaled_keys, v_heads, preferred_element_type=jnp.float32)
    carried = carried_state(last, summary, "ctx")
    inter = jnp.exp(cum)[:, :, None] * jnp.einsum(
        "thd,hde->the", q_heads.astype(jnp.float32), carried, precision=lax.Precision.HIGHEST
    )
    attn = intra + inter
    normed = (
        (attn * lax.rsqrt(jnp.mean(attn * attn, axis=-1, keepdims=True) + EPS))
        .astype(jnp.bfloat16)
        .reshape(tok, heads_here * head_dim)
    )
    n_exp = lax.axis_size("exp")
    proj = lax.psum_scatter(
        jnp.dot(normed, out_proj, preferred_element_type=jnp.float32).astype(jnp.bfloat16),
        "exp",
        scatter_dimension=0,
        tiled=True,
    ).astype(jnp.float32)
    feature_vector = residual.astype(jnp.float32) + proj
    moe_in = (
        feature_vector
        * lax.rsqrt(jnp.mean(feature_vector * feature_vector, axis=-1, keepdims=True) + EPS)
    ).astype(jnp.bfloat16)
    local_experts = w_gate.shape[0]
    experts = local_experts * n_exp
    mtok = residual.shape[0]
    width = residual.shape[1]
    capacity = max(2, (5 * mtok + 2 * experts - 1) // (2 * experts))
    total_slots = experts * capacity
    local_slot_table = slot_table(expert_ids, capacity, local_experts, experts)
    packed = jnp.dot(
        dispatch_table(local_slot_table, total_slots), moe_in, preferred_element_type=jnp.float32
    ).astype(jnp.bfloat16)
    packed = packed.reshape(n_exp, capacity, local_experts, width)
    arrived = lax.all_to_all(packed, "exp", split_axis=0, concat_axis=1, tiled=True).reshape(
        n_exp * capacity, local_experts, width
    )
    piece = lax.all_gather(arrived, "ctx", axis=0, tiled=True)
    hidden_units = w_gate.shape[2]
    both = jnp.einsum(
        "red,edf->ref",
        piece,
        jnp.concatenate([w_gate, w_up], axis=2),
        preferred_element_type=jnp.float32,
    )
    gate = both[:, :, :hidden_units]
    upper = both[:, :, hidden_units:]
    acts = (jax.nn.silu(gate) * upper).astype(jnp.bfloat16)
    summed = lax.psum_scatter(
        jnp.einsum("ref,efd->red", acts, w_down, preferred_element_type=jnp.float32).astype(
            jnp.bfloat16
        ),
        "ctx",
        scatter_dimension=0,
        tiled=True,
    )
    outgoing = summed.reshape(n_exp, capacity, local_experts, width)
    returned = lax.all_to_all(outgoing, "exp", split_axis=0, concat_axis=0, tiled=True).reshape(
        total_slots, width
    )
    picker = (
        local_slot_table.reshape(-1)[:, None] == jnp.arange(total_slots, dtype=jnp.int32)[None, :]
    ).astype(jnp.bfloat16)
    fetched = jnp.dot(picker, returned, preferred_element_type=jnp.float32).reshape(mtok, 2, width)
    moe = route_weights[:, 0:1] * fetched[:, 0] + route_weights[:, 1:2] * fetched[:, 1]
    return (feature_vector + moe).astype(jnp.bfloat16)


def solution(mesh):
    placed = (
        P("ctx", "exp"),
        P("ctx", "exp"),
        P("ctx", "exp"),
        P("ctx", "exp"),
        P(("ctx", "exp"), None),
        P("exp", None),
        P(("ctx", "exp"), None),
        P(("ctx", "exp"), None),
        P("exp", None, "ctx"),
        P("exp", None, "ctx"),
        P("exp", "ctx", None),
    )
    return jax.shard_map(
        on_device, mesh=mesh, in_specs=placed, out_specs=P(("ctx", "exp"), None), check_vma=False
    )
```

```python
import jax
import jax.numpy as jnp
from jax import lax
from jax.sharding import PartitionSpec as P

EPS = 1e-06


def pack(rate, state):
    heads, hd, _ = state.shape
    hi = rate.astype(jnp.bfloat16)
    lo = (rate - hi.astype(jnp.float32)).astype(jnp.bfloat16)
    lane = jnp.arange(hd, dtype=jnp.int32)[None, :]
    rate_row = jnp.where(lane == 0, hi[:, None], jnp.where(lane == 1, lo[:, None], 0.0)).astype(
        jnp.bfloat16
    )
    return jnp.concatenate([state.astype(jnp.bfloat16).reshape(heads, hd * hd), rate_row], axis=1)


def unpack(payload, hd):
    heads = payload.shape[0]
    state = payload[:, : hd * hd].astype(jnp.float32).reshape(heads, hd, hd)
    rate = payload[:, hd * hd].astype(jnp.float32) + payload[:, hd * hd + 1].astype(jnp.float32)
    return rate, state


def carried_state(last, summary, axis, tied):
    length = lax.axis_size(axis)
    hd = summary.shape[1]
    incl_r, incl_s = last, summary
    excl_r, excl_s = jnp.zeros_like(last), jnp.zeros_like(summary)
    shift = 1
    while shift < length:
        pairs = [(i, i + shift) for i in range(length - shift)]
        sent = pack(incl_r, incl_s)
        if shift == 2:
            tied, sent = lax.optimization_barrier((tied, sent))
        in_r, in_s = unpack(lax.ppermute(sent, axis, pairs), hd)
        excl_s = jnp.exp(excl_r)[:, None, None] * in_s + excl_s
        excl_r = in_r + excl_r
        if 2 * shift < length:
            incl_s = jnp.exp(incl_r)[:, None, None] * in_s + incl_s
            incl_r = in_r + incl_r
        shift *= 2
    return excl_s, tied


def slot_table(chosen_specialist_index, capacity, local_experts, experts):
    flat = chosen_specialist_index.reshape(-1)
    onehot = (flat[:, None] == jnp.arange(experts, dtype=jnp.int32)[None, :]).astype(jnp.int32)
    preceding_sum = jnp.cumsum(onehot, axis=0) - onehot
    position = jnp.sum(preceding_sum * onehot, axis=1)
    slots = (
        flat // local_experts * (capacity * local_experts)
        + position * local_experts
        + flat % local_experts
    )
    return slots.reshape(chosen_specialist_index.shape)


def dispatch_table(slots, total_slots):
    assignment_tally = slots[None, :, :] == jnp.arange(total_slots, dtype=jnp.int32)[:, None, None]
    return jnp.any(assignment_tally, axis=2).astype(jnp.bfloat16)


def on_device(
    queries,
    keys,
    values,
    log_decay,
    residual,
    out_proj,
    expert_ids,
    route_weights,
    w_gate,
    w_up,
    w_down,
):
    tok = queries.shape[0]
    heads_here = log_decay.shape[1]
    head_dim = queries.shape[1] // heads_here
    q_heads = queries.reshape(tok, heads_here, head_dim)
    k_heads = keys.reshape(tok, heads_here, head_dim)
    v_heads = values.reshape(tok, heads_here, head_dim)
    place = jnp.arange(tok, dtype=jnp.int32)
    lower = (place[:, None] >= place[None, :]).astype(jnp.float32)
    cum = jnp.dot(lower, log_decay, precision=lax.Precision.HIGHEST)
    scores = jnp.einsum("thd,shd->hts", q_heads, k_heads, preferred_element_type=jnp.float32)
    causal = (place[:, None] >= place[None, :])[None]
    diff = cum.T[:, :, None] - cum.T[:, None, :]
    weights = jnp.where(causal, scores * jnp.exp(jnp.where(causal, diff, 0.0)), 0.0).astype(
        jnp.bfloat16
    )
    intra = jnp.einsum("hts,shd->thd", weights, v_heads, preferred_element_type=jnp.float32)
    last = cum[-1]
    scaled_keys = (k_heads.astype(jnp.float32) * jnp.exp(last[None, :] - cum)[:, :, None]).astype(
        jnp.bfloat16
    )
    summary = jnp.einsum("thd,the->hde", scaled_keys, v_heads, preferred_element_type=jnp.float32)
    carried, intra = carried_state(last, summary, "ctx", intra)
    inter = jnp.exp(cum)[:, :, None] * jnp.einsum(
        "thd,hde->the", q_heads.astype(jnp.float32), carried, precision=lax.Precision.HIGHEST
    )
    attn = intra + inter
    normed = (
        (attn * lax.rsqrt(jnp.mean(attn * attn, axis=-1, keepdims=True) + EPS))
        .astype(jnp.bfloat16)
        .reshape(tok, heads_here * head_dim)
    )
    n_exp = lax.axis_size("exp")
    proj = lax.psum_scatter(
        jnp.dot(normed, out_proj, preferred_element_type=jnp.float32).astype(jnp.bfloat16),
        "exp",
        scatter_dimension=0,
        tiled=True,
    ).astype(jnp.float32)
    feature_vector = residual.astype(jnp.float32) + proj
    moe_in = (
        feature_vector
        * lax.rsqrt(jnp.mean(feature_vector * feature_vector, axis=-1, keepdims=True) + EPS)
    ).astype(jnp.bfloat16)
    local_experts = w_gate.shape[0]
    experts = local_experts * n_exp
    mtok = residual.shape[0]
    width = residual.shape[1]
    capacity = max(2, (5 * mtok + 2 * experts - 1) // (2 * experts))
    total_slots = experts * capacity
    local_slot_table = slot_table(expert_ids, capacity, local_experts, experts)
    packed = jnp.dot(
        dispatch_table(local_slot_table, total_slots), moe_in, preferred_element_type=jnp.float32
    ).astype(jnp.bfloat16)
    packed = packed.reshape(n_exp, capacity, local_experts, width)
    arrived = lax.all_to_all(packed, "exp", split_axis=0, concat_axis=1, tiled=True).reshape(
        n_exp * capacity, local_experts, width
    )
    piece = lax.all_gather(arrived, "ctx", axis=0, tiled=True)
    hidden_units = w_gate.shape[2]
    both = jnp.einsum(
        "red,edf->ref",
        piece,
        jnp.concatenate([w_gate, w_up], axis=2),
        preferred_element_type=jnp.float32,
    )
    gate = both[:, :, :hidden_units]
    upper = both[:, :, hidden_units:]
    acts = (jax.nn.silu(gate) * upper).astype(jnp.bfloat16)
    summed = lax.psum_scatter(
        jnp.einsum("ref,efd->red", acts, w_down, preferred_element_type=jnp.float32).astype(
            jnp.bfloat16
        ),
        "ctx",
        scatter_dimension=0,
        tiled=True,
    )
    outgoing = summed.reshape(n_exp, capacity, local_experts, width)
    returned = lax.all_to_all(outgoing, "exp", split_axis=0, concat_axis=0, tiled=True).reshape(
        total_slots, width
    )
    picker = (
        local_slot_table.reshape(-1)[:, None] == jnp.arange(total_slots, dtype=jnp.int32)[None, :]
    ).astype(jnp.bfloat16)
    fetched = jnp.dot(picker, returned, preferred_element_type=jnp.float32).reshape(mtok, 2, width)
    moe = route_weights[:, 0:1] * fetched[:, 0] + route_weights[:, 1:2] * fetched[:, 1]
    return (feature_vector + moe).astype(jnp.bfloat16)


def solution(mesh):
    placed = (
        P("ctx", "exp"),
        P("ctx", "exp"),
        P("ctx", "exp"),
        P("ctx", "exp"),
        P(("ctx", "exp"), None),
        P("exp", None),
        P(("ctx", "exp"), None),
        P(("ctx", "exp"), None),
        P("exp", None, "ctx"),
        P("exp", None, "ctx"),
        P("exp", "ctx", None),
    )
    return jax.shard_map(
        on_device, mesh=mesh, in_specs=placed, out_specs=P(("ctx", "exp"), None), check_vma=False
    )
```

```python
import jax
import jax.numpy as jnp
from jax import lax
from jax.sharding import PartitionSpec as P

EPS = 1e-06


def pack(rate, state):
    heads, hd, _ = state.shape
    hi = rate.astype(jnp.bfloat16)
    lo = (rate - hi.astype(jnp.float32)).astype(jnp.bfloat16)
    lane = jnp.arange(hd, dtype=jnp.int32)[None, :]
    rate_row = jnp.where(lane == 0, hi[:, None], jnp.where(lane == 1, lo[:, None], 0.0)).astype(
        jnp.bfloat16
    )
    return jnp.concatenate([state.astype(jnp.bfloat16).reshape(heads, hd * hd), rate_row], axis=1)


def unpack(payload, hd):
    heads = payload.shape[0]
    state = payload[:, : hd * hd].astype(jnp.float32).reshape(heads, hd, hd)
    rate = payload[:, hd * hd].astype(jnp.float32) + payload[:, hd * hd + 1].astype(jnp.float32)
    return rate, state


def carried_state(last, summary, axis, tied):
    length = lax.axis_size(axis)
    hd = summary.shape[1]
    incl_r, incl_s = last, summary
    excl_r, excl_s = jnp.zeros_like(last), jnp.zeros_like(summary)
    shift = 1
    while shift < length:
        pairs = [(i, i + shift) for i in range(length - shift)]
        sent = pack(incl_r, incl_s)
        if shift == 2:
            tied, sent = lax.optimization_barrier((tied, sent))
        in_r, in_s = unpack(lax.ppermute(sent, axis, pairs), hd)
        excl_s = jnp.exp(excl_r)[:, None, None] * in_s + excl_s
        excl_r = in_r + excl_r
        if 2 * shift < length:
            incl_s = jnp.exp(incl_r)[:, None, None] * in_s + incl_s
            incl_r = in_r + incl_r
        shift *= 2
    return excl_s, tied


def slot_table(chosen_specialist_index, capacity, local_experts, experts):
    flat = chosen_specialist_index.reshape(-1)
    onehot = (flat[:, None] == jnp.arange(experts, dtype=jnp.int32)[None, :]).astype(jnp.int32)
    preceding_sum = jnp.cumsum(onehot, axis=0) - onehot
    position = jnp.sum(preceding_sum * onehot, axis=1)
    slots = (
        flat // local_experts * (capacity * local_experts)
        + position * local_experts
        + flat % local_experts
    )
    return slots.reshape(chosen_specialist_index.shape)


def dispatch_table(slots, total_slots):
    assignment_tally = slots[None, :, :] == jnp.arange(total_slots, dtype=jnp.int32)[:, None, None]
    return jnp.any(assignment_tally, axis=2).astype(jnp.bfloat16)


def on_device(
    queries,
    keys,
    values,
    log_decay,
    residual,
    out_proj,
    expert_ids,
    route_weights,
    w_gate,
    w_up,
    w_down,
):
    tok = queries.shape[0]
    heads_here = log_decay.shape[1]
    head_dim = queries.shape[1] // heads_here
    q_heads = queries.reshape(tok, heads_here, head_dim)
    k_heads = keys.reshape(tok, heads_here, head_dim)
    v_heads = values.reshape(tok, heads_here, head_dim)
    place = jnp.arange(tok, dtype=jnp.int32)
    lower = (place[:, None] >= place[None, :]).astype(jnp.float32)
    cum = jnp.dot(lower, log_decay, precision=lax.Precision.HIGHEST)
    scores = jnp.einsum("thd,shd->hts", q_heads, k_heads, preferred_element_type=jnp.float32)
    causal = (place[:, None] >= place[None, :])[None]
    diff = cum.T[:, :, None] - cum.T[:, None, :]
    weights = jnp.where(causal, scores * jnp.exp(jnp.where(causal, diff, 0.0)), 0.0).astype(
        jnp.bfloat16
    )
    last = cum[-1]
    scaled_keys = (k_heads.astype(jnp.float32) * jnp.exp(last[None, :] - cum)[:, :, None]).astype(
        jnp.bfloat16
    )
    summary = jnp.einsum("thd,the->hde", scaled_keys, v_heads, preferred_element_type=jnp.float32)
    carried, weights = carried_state(last, summary, "ctx", weights)
    intra = jnp.einsum("hts,shd->thd", weights, v_heads, preferred_element_type=jnp.float32)
    inter = jnp.exp(cum)[:, :, None] * jnp.einsum(
        "thd,hde->the", q_heads.astype(jnp.float32), carried, precision=lax.Precision.HIGHEST
    )
    attn = intra + inter
    normed = (
        (attn * lax.rsqrt(jnp.mean(attn * attn, axis=-1, keepdims=True) + EPS))
        .astype(jnp.bfloat16)
        .reshape(tok, heads_here * head_dim)
    )
    n_exp = lax.axis_size("exp")
    proj = lax.psum_scatter(
        jnp.dot(normed, out_proj, preferred_element_type=jnp.float32).astype(jnp.bfloat16),
        "exp",
        scatter_dimension=0,
        tiled=True,
    ).astype(jnp.float32)
    feature_vector = residual.astype(jnp.float32) + proj
    moe_in = (
        feature_vector
        * lax.rsqrt(jnp.mean(feature_vector * feature_vector, axis=-1, keepdims=True) + EPS)
    ).astype(jnp.bfloat16)
    local_experts = w_gate.shape[0]
    experts = local_experts * n_exp
    mtok = residual.shape[0]
    width = residual.shape[1]
    capacity = max(2, (5 * mtok + 2 * experts - 1) // (2 * experts))
    total_slots = experts * capacity
    local_slot_table = slot_table(expert_ids, capacity, local_experts, experts)
    packed = jnp.dot(
        dispatch_table(local_slot_table, total_slots), moe_in, preferred_element_type=jnp.float32
    ).astype(jnp.bfloat16)
    packed = packed.reshape(n_exp, capacity, local_experts, width)
    arrived = lax.all_to_all(packed, "exp", split_axis=0, concat_axis=1, tiled=True).reshape(
        n_exp * capacity, local_experts, width
    )
    piece = lax.all_gather(arrived, "ctx", axis=0, tiled=True)
    hidden_units = w_gate.shape[2]
    both = jnp.einsum(
        "red,edf->ref",
        piece,
        jnp.concatenate([w_gate, w_up], axis=2),
        preferred_element_type=jnp.float32,
    )
    gate = both[:, :, :hidden_units]
    upper = both[:, :, hidden_units:]
    acts = (jax.nn.silu(gate) * upper).astype(jnp.bfloat16)
    summed = lax.psum_scatter(
        jnp.einsum("ref,efd->red", acts, w_down, preferred_element_type=jnp.float32).astype(
            jnp.bfloat16
        ),
        "ctx",
        scatter_dimension=0,
        tiled=True,
    )
    outgoing = summed.reshape(n_exp, capacity, local_experts, width)
    returned = lax.all_to_all(outgoing, "exp", split_axis=0, concat_axis=0, tiled=True).reshape(
        total_slots, width
    )
    picker = (
        local_slot_table.reshape(-1)[:, None] == jnp.arange(total_slots, dtype=jnp.int32)[None, :]
    ).astype(jnp.bfloat16)
    fetched = jnp.dot(picker, returned, preferred_element_type=jnp.float32).reshape(mtok, 2, width)
    moe = route_weights[:, 0:1] * fetched[:, 0] + route_weights[:, 1:2] * fetched[:, 1]
    return (feature_vector + moe).astype(jnp.bfloat16)


def solution(mesh):
    placed = (
        P("ctx", "exp"),
        P("ctx", "exp"),
        P("ctx", "exp"),
        P("ctx", "exp"),
        P(("ctx", "exp"), None),
        P("exp", None),
        P(("ctx", "exp"), None),
        P(("ctx", "exp"), None),
        P("exp", None, "ctx"),
        P("exp", None, "ctx"),
        P("exp", "ctx", None),
    )
    return jax.shard_map(
        on_device, mesh=mesh, in_specs=placed, out_specs=P(("ctx", "exp"), None), check_vma=False
    )
```

```python
import jax
import jax.numpy as jnp
from jax import lax
from jax.sharding import PartitionSpec as P

EPS = 1e-06


def pack(rate, state):
    heads, hd, _ = state.shape
    hi = rate.astype(jnp.bfloat16)
    lo = (rate - hi.astype(jnp.float32)).astype(jnp.bfloat16)
    row = jnp.arange(16, dtype=jnp.int32)[None, :, None]
    rate_rows = jnp.where(row == 0, hi[:, None, None], jnp.where(row == 1, lo[:, None, None], 0.0))
    rate_rows = jnp.broadcast_to(rate_rows, (heads, 16, hd)).astype(jnp.bfloat16)
    return jnp.concatenate([state.astype(jnp.bfloat16), rate_rows], axis=1)


def unpack(payload, hd):
    state = payload[:, :hd, :].astype(jnp.float32)
    rate = payload[:, hd, 0].astype(jnp.float32) + payload[:, hd + 1, 0].astype(jnp.float32)
    return rate, state


def carried_state(last, summary, axis):
    length = lax.axis_size(axis)
    hd = summary.shape[1]
    incl_r, incl_s = last, summary
    excl_r, excl_s = jnp.zeros_like(last), jnp.zeros_like(summary)
    shift = 1
    while shift < length:
        pairs = [(i, i + shift) for i in range(length - shift)]
        in_r, in_s = unpack(lax.ppermute(pack(incl_r, incl_s), axis, pairs), hd)
        excl_s = jnp.exp(excl_r)[:, None, None] * in_s + excl_s
        excl_r = in_r + excl_r
        if 2 * shift < length:
            incl_s = jnp.exp(incl_r)[:, None, None] * in_s + incl_s
            incl_r = in_r + incl_r
        shift *= 2
    return excl_s


def slot_table(chosen_specialist_index, capacity, local_experts, experts):
    flat = chosen_specialist_index.reshape(-1)
    onehot = (flat[:, None] == jnp.arange(experts, dtype=jnp.int32)[None, :]).astype(jnp.int32)
    preceding_sum = jnp.cumsum(onehot, axis=0) - onehot
    position = jnp.sum(preceding_sum * onehot, axis=1)
    slots = (
        flat // local_experts * (capacity * local_experts)
        + position * local_experts
        + flat % local_experts
    )
    return slots.reshape(chosen_specialist_index.shape)


def dispatch_table(slots, total_slots):
    assignment_tally = slots[None, :, :] == jnp.arange(total_slots, dtype=jnp.int32)[:, None, None]
    return jnp.any(assignment_tally, axis=2).astype(jnp.bfloat16)


def on_device(
    queries,
    keys,
    values,
    log_decay,
    residual,
    out_proj,
    expert_ids,
    route_weights,
    w_gate,
    w_up,
    w_down,
):
    tok = queries.shape[0]
    heads_here = log_decay.shape[1]
    head_dim = queries.shape[1] // heads_here
    q_heads = queries.reshape(tok, heads_here, head_dim)
    k_heads = keys.reshape(tok, heads_here, head_dim)
    v_heads = values.reshape(tok, heads_here, head_dim)
    place = jnp.arange(tok, dtype=jnp.int32)
    lower = (place[:, None] >= place[None, :]).astype(jnp.float32)
    cum = jnp.dot(lower, log_decay, precision=lax.Precision.HIGHEST)
    scores = jnp.einsum("thd,shd->hts", q_heads, k_heads, preferred_element_type=jnp.float32)
    causal = (place[:, None] >= place[None, :])[None]
    diff = cum.T[:, :, None] - cum.T[:, None, :]
    weights = jnp.where(causal, scores * jnp.exp(jnp.where(causal, diff, 0.0)), 0.0).astype(
        jnp.bfloat16
    )
    intra = jnp.einsum("hts,shd->thd", weights, v_heads, preferred_element_type=jnp.float32)
    last = cum[-1]
    scaled_keys = (k_heads.astype(jnp.float32) * jnp.exp(last[None, :] - cum)[:, :, None]).astype(
        jnp.bfloat16
    )
    summary = jnp.einsum("thd,the->hde", scaled_keys, v_heads, preferred_element_type=jnp.float32)
    carried = carried_state(last, summary, "ctx")
    inter = jnp.exp(cum)[:, :, None] * jnp.einsum(
        "thd,hde->the", q_heads.astype(jnp.float32), carried, precision=lax.Precision.HIGHEST
    )
    attn = intra + inter
    normed = (
        (attn * lax.rsqrt(jnp.mean(attn * attn, axis=-1, keepdims=True) + EPS))
        .astype(jnp.bfloat16)
        .reshape(tok, heads_here * head_dim)
    )
    n_exp = lax.axis_size("exp")
    proj = lax.psum_scatter(
        jnp.dot(normed, out_proj, preferred_element_type=jnp.float32).astype(jnp.bfloat16),
        "exp",
        scatter_dimension=0,
        tiled=True,
    ).astype(jnp.float32)
    feature_vector = residual.astype(jnp.float32) + proj
    moe_in = (
        feature_vector
        * lax.rsqrt(jnp.mean(feature_vector * feature_vector, axis=-1, keepdims=True) + EPS)
    ).astype(jnp.bfloat16)
    local_experts = w_gate.shape[0]
    experts = local_experts * n_exp
    mtok = residual.shape[0]
    width = residual.shape[1]
    capacity = max(2, (5 * mtok + 2 * experts - 1) // (2 * experts))
    total_slots = experts * capacity
    local_slot_table = slot_table(expert_ids, capacity, local_experts, experts)
    packed = jnp.dot(
        dispatch_table(local_slot_table, total_slots), moe_in, preferred_element_type=jnp.float32
    ).astype(jnp.bfloat16)
    packed = packed.reshape(n_exp, capacity, local_experts, width)
    arrived = lax.all_to_all(packed, "exp", split_axis=0, concat_axis=1, tiled=True).reshape(
        n_exp * capacity, local_experts, width
    )
    piece = lax.all_gather(arrived, "ctx", axis=0, tiled=True)
    hidden_units = w_gate.shape[2]
    both = jnp.einsum(
        "red,edf->ref",
        piece,
        jnp.concatenate([w_gate, w_up], axis=2),
        preferred_element_type=jnp.float32,
    )
    gate = both[:, :, :hidden_units]
    upper = both[:, :, hidden_units:]
    acts = (jax.nn.silu(gate) * upper).astype(jnp.bfloat16)
    summed = lax.psum_scatter(
        jnp.einsum("ref,efd->red", acts, w_down, preferred_element_type=jnp.float32).astype(
            jnp.bfloat16
        ),
        "ctx",
        scatter_dimension=0,
        tiled=True,
    )
    outgoing = summed.reshape(n_exp, capacity, local_experts, width)
    returned = lax.all_to_all(outgoing, "exp", split_axis=0, concat_axis=0, tiled=True).reshape(
        total_slots, width
    )
    picker = (
        local_slot_table.reshape(-1)[:, None] == jnp.arange(total_slots, dtype=jnp.int32)[None, :]
    ).astype(jnp.bfloat16)
    fetched = jnp.dot(picker, returned, preferred_element_type=jnp.float32).reshape(mtok, 2, width)
    moe = route_weights[:, 0:1] * fetched[:, 0] + route_weights[:, 1:2] * fetched[:, 1]
    return (feature_vector + moe).astype(jnp.bfloat16)


def solution(mesh):
    placed = (
        P("ctx", "exp"),
        P("ctx", "exp"),
        P("ctx", "exp"),
        P("ctx", "exp"),
        P(("ctx", "exp"), None),
        P("exp", None),
        P(("ctx", "exp"), None),
        P(("ctx", "exp"), None),
        P("exp", None, "ctx"),
        P("exp", None, "ctx"),
        P("exp", "ctx", None),
    )
    return jax.shard_map(
        on_device, mesh=mesh, in_specs=placed, out_specs=P(("ctx", "exp"), None), check_vma=False
    )
```
